32 devices in a mesh: row: 8 (over z, core), col: 4 (over y, x).
Axes of the slice: x: 2, y: 2, z: 4, core: 2. Of those that a mesh axis runs over, the one named last changes fastest.
Arguments:
- activations: bfloat16 [1024, 8192], P('col', 'row'), may hold values from -6 to 6
- out_grad: bfloat16 [1024, 8192], P('col', 'row'), may hold values from -6 to 6
- gate_pre: bfloat16 [1024, 16384], P('row', 'col'), may hold values from -8 to 8
- up_proj: bfloat16 [1024, 16384], P('row', 'col'), may hold values from -6 to 6
- gate_weight: bfloat16 [8192, 16384], P('row', 'col'), may hold values from -0.0625 to 0.0625
- up_weight: bfloat16 [8192, 16384], P('row', 'col'), may hold values from -0.0625 to 0.0625
- down_weight: bfloat16 [16384, 8192], P('col', 'row'), may hold values from -0.046875 to 0.046875
Outputs:
- input_grad: bfloat16 [1024, 8192], P('col', 'row')
- gate_grad: bfloat16 [8192, 16384], P('row', 'col')
- up_grad: bfloat16 [8192, 16384], P('row', 'col')
- down_grad: bfloat16 [16384, 8192], P('col', 'row')
The draws below stay inside these ranges and needn't reach their ends.
All inputs are finite; a program needn't handle non-finite values.
Results may differ from the reference program's by a relative error of at most 0.0051.
Values may be sent and summed in bfloat16 or wider, within the bound.
No kernel may reach another device: no remote copies, remote signals or barrier semaphores. Data moves between devices by JAX's collectives and lax.ppermute only.
A program may use at most 192 MiB of HBM per device.

```python
import jax
import jax.numpy as jnp
from jax import lax

D = 8192
FF = 16384
TOKENS = 1024


def block_levels(key, dims, cuts, least, top_value):
    level = 1.0
    for dim, parts in cuts:
        heights = jax.random.uniform(jax.random.fold_in(jax.random.fold_in(key, 6), dim), (parts,), jnp.float32, least / len(cuts), top_value / len(cuts))
        level = level * jnp.repeat(jnp.exp(heights), dims[dim] // parts).reshape((-1,) + (1,) * (len(dims) - 1 - dim))
    return level


def bell_draw(rng, dims, scale, bound, pieces=(), dtype=jnp.bfloat16):
    entries = jax.random.normal(rng, dims, jnp.float32) * scale
    if len(pieces) > 0:
        entries = block_levels(rng, dims, pieces, -0.22, 0.18) * entries
    return jnp.clip(entries, min=-bound, max=bound).astype(dtype)


def setup_inputs(seed: int = 0) -> dict:
    arg_keys = jax.random.split(jax.random.key(seed), 8)
    activations = bell_draw(arg_keys[0], (TOKENS, D), 1.0, 6.0, ((0, 4), (1, 8)))
    out_grad = bell_draw(arg_keys[1], (TOKENS, D), 1.0, 6.0, ((0, 4), (1, 8)))
    gate_pre = bell_draw(arg_keys[2], (TOKENS, FF), 1.5, 8.0, ((0, 8), (1, 4)))
    up_proj = bell_draw(arg_keys[3], (TOKENS, FF), 1.0, 6.0, ((0, 8), (1, 4)))
    gate_weight = bell_draw(arg_keys[4], (D, FF), D ** -0.5, 0.0625, ((0, 8), (1, 4)))
    up_weight = bell_draw(arg_keys[5], (D, FF), D ** -0.5, 0.0625, ((0, 8), (1, 4)))
    down_weight = bell_draw(arg_keys[6], (FF, D), FF ** -0.5, 0.046875, ((0, 4), (1, 8)))
    return {"activations": activations, "out_grad": out_grad, "gate_pre": gate_pre, "up_proj": up_proj, "gate_weight": gate_weight, "up_weight": up_weight, "down_weight": down_weight}


def reference(activations, out_grad, gate_pre, up_proj, gate_weight, up_weight, down_weight):
    contract_last = (((1,), (1,)), ((), ()))
    contract_first = (((0,), (0,)), ((), ()))
    hid_grad = lax.dot_general(out_grad, down_weight, contract_last, preferred_element_type=jnp.float32)
    gate_float = gate_pre.astype(jnp.float32)
    up_float = up_proj.astype(jnp.float32)
    sigmoid_gate = jax.nn.sigmoid(gate_float)
    silu_gate = gate_float * sigmoid_gate
    hidden_act = (silu_gate * up_float).astype(jnp.bfloat16)
    gate_delta = (hid_grad * up_float * sigmoid_gate * (1.0 + gate_float * (1.0 - sigmoid_gate))).astype(jnp.bfloat16)
    up_delta = (hid_grad * silu_gate).astype(jnp.bfloat16)
    input_grad = lax.dot_general(gate_delta, gate_weight, contract_last, preferred_element_type=jnp.float32)
    input_grad = input_grad + lax.dot_general(up_delta, up_weight, contract_last, preferred_element_type=jnp.float32)
    factor = float(TOKENS) ** -0.5
    gate_grad = lax.dot_general(activations, gate_delta, contract_first, preferred_element_type=jnp.float32) * factor
    up_grad = lax.dot_general(activations, up_delta, contract_first, preferred_element_type=jnp.float32) * factor
    down_grad = lax.dot_general(hidden_act, out_grad, contract_first, preferred_element_type=jnp.float32) * factor
    return (input_grad.astype(jnp.bfloat16), gate_grad.astype(jnp.bfloat16), up_grad.astype(jnp.bfloat16), down_grad.astype(jnp.bfloat16))
```

```python
import jax
import jax.numpy as jnp
from jax import lax
from jax.sharding import PartitionSpec as P


CONTRACT_LAST = (((1,), (1,)), ((), ()))
CONTRACT_FIRST = (((0,), (0,)), ((), ()))
ROW = ("z", "core")


def body(activations, out_grad, gate_pre, up_proj, gate_weight, up_weight, down_weight):
    gate_float = gate_pre.astype(jnp.float32)
    up_float = up_proj.astype(jnp.float32)
    sigmoid_gate = jax.nn.sigmoid(gate_float)
    silu_gate = gate_float * sigmoid_gate
    hidden_local = (silu_gate * up_float).astype(jnp.bfloat16)
    hidden_act = lax.all_gather(hidden_local, ROW, axis=0, tiled=True)

    grad_full = lax.all_gather(out_grad, "col", axis=0, tiled=True)
    act_full = lax.all_gather(activations, "col", axis=0, tiled=True)
    tokens_all = act_full.shape[0]

    hid_partial = lax.dot_general(
        grad_full, down_weight, CONTRACT_LAST, preferred_element_type=jnp.float32
    )
    hid_partial, hidden_act = lax.optimization_barrier((hid_partial, hidden_act))
    chips = lax.axis_size("z")
    hid_partial = hid_partial.reshape(chips, 2, -1, hid_partial.shape[1])
    hid_partial = jnp.swapaxes(hid_partial, 0, 1)
    hid_pair = lax.psum_scatter(hid_partial, "core", scatter_dimension=0, tiled=True)[0]
    hid_rows = lax.psum_scatter(
        hid_pair.astype(jnp.bfloat16), "z", scatter_dimension=0, tiled=True
    )[0].astype(jnp.float32)
    gate_local = (
        hid_rows * up_float * sigmoid_gate * (1.0 + gate_float * (1.0 - sigmoid_gate))
    ).astype(jnp.bfloat16)
    up_local = (hid_rows * silu_gate).astype(jnp.bfloat16)

    acc_down = lax.dot_general(
        hidden_act, grad_full, CONTRACT_FIRST, preferred_element_type=jnp.float32
    )
    gate_delta = lax.all_gather(gate_local, ROW, axis=0, tiled=True)
    up_delta = lax.all_gather(up_local, ROW, axis=0, tiled=True)
    acc_gate = lax.dot_general(
        act_full, gate_delta, CONTRACT_FIRST, preferred_element_type=jnp.float32
    )
    acc_up = lax.dot_general(act_full, up_delta, CONTRACT_FIRST, preferred_element_type=jnp.float32)
    input_rows = lax.dot_general(
        gate_delta, gate_weight, CONTRACT_LAST, preferred_element_type=jnp.float32
    )
    input_rows = input_rows + lax.dot_general(
        up_delta, up_weight, CONTRACT_LAST, preferred_element_type=jnp.float32
    )
    input_rows = lax.psum_scatter(input_rows, "col", scatter_dimension=0, tiled=True).astype(
        jnp.bfloat16
    )
    factor = float(tokens_all) ** (-0.5)
    return (
        input_rows,
        (acc_gate * factor).astype(jnp.bfloat16),
        (acc_up * factor).astype(jnp.bfloat16),
        (acc_down * factor).astype(jnp.bfloat16),
    )


def solution(mesh):
    in_specs = (
        P("col", ROW),
        P("col", ROW),
        P(ROW, "col"),
        P(ROW, "col"),
        P(ROW, "col"),
        P(ROW, "col"),
        P("col", ROW),
    )
    out_specs = (P("col", ROW), P(ROW, "col"), P(ROW, "col"), P("col", ROW))
    devices = mesh.devices.reshape(mesh.shape["row"] // 2, 2, mesh.shape["col"])
    split_mesh = jax.sharding.Mesh(devices, ("z", "core", "col"))
    return jax.shard_map(body, mesh=split_mesh, in_specs=in_specs, out_specs=out_specs, check_vma=False)
```

```python
import jax
import jax.numpy as jnp
from jax import lax
from jax.sharding import PartitionSpec as P


CONTRACT_LAST = (((1,), (1,)), ((), ()))
CONTRACT_FIRST = (((0,), (0,)), ((), ()))
ROW = ("z", "core")


def shift_perm(n, s):
    return [(i, (i + s) % n) for i in range(n)]


def gather_col(block):
    n = lax.axis_size("col")
    c = lax.axis_index("col")
    rows = block.shape[0]
    full = jnp.zeros((n * rows,) + block.shape[1:], block.dtype)
    full = lax.dynamic_update_slice_in_dim(full, block, c * rows, axis=0)
    for s in range(1, n):
        part = lax.ppermute(block, "col", shift_perm(n, s))
        full = lax.dynamic_update_slice_in_dim(full, part, ((c - s) % n) * rows, axis=0)
    return full


def reduce_scatter_col(partial):
    n = lax.axis_size("col")
    c = lax.axis_index("col")
    blocks = partial.reshape((n, -1) + partial.shape[1:])
    total = lax.dynamic_index_in_dim(blocks, c, axis=0, keepdims=False)
    for s in range(1, n):
        piece = lax.dynamic_index_in_dim(blocks, (c + s) % n, axis=0, keepdims=False)
        total = total + lax.ppermute(piece, "col", shift_perm(n, s))
    return total


def body(activations, out_grad, gate_pre, up_proj, gate_weight, up_weight, down_weight):
    gate_float = gate_pre.astype(jnp.float32)
    up_float = up_proj.astype(jnp.float32)
    sigmoid_gate = jax.nn.sigmoid(gate_float)
    silu_gate = gate_float * sigmoid_gate
    hidden_local = (silu_gate * up_float).astype(jnp.bfloat16)
    hidden_act = lax.all_gather(hidden_local, ROW, axis=0, tiled=True)

    grad_full = gather_col(out_grad)
    act_full = gather_col(activations)
    tokens_all = act_full.shape[0]

    chips = lax.axis_size("z")
    z = lax.axis_index("z")
    core = lax.axis_index("core")
    width = grad_full.shape[1]
    grad_blocks = grad_full.reshape(chips, 2, -1, width)
    grad_send = lax.dynamic_index_in_dim(grad_blocks, 1 - core, axis=1, keepdims=False)
    grad_keep = lax.dynamic_index_in_dim(grad_blocks, core, axis=1, keepdims=False)
    hid_send = lax.dot_general(
        grad_send.reshape(-1, width), down_weight, CONTRACT_LAST,
        preferred_element_type=jnp.float32,
    )
    hid_recv = lax.ppermute(hid_send, "core", [(0, 1), (1, 0)])
    hid_keep = lax.dot_general(
        grad_keep.reshape(-1, width), down_weight, CONTRACT_LAST,
        preferred_element_type=jnp.float32,
    )
    chip_sum = (hid_keep + hid_recv).reshape(chips, -1, hid_keep.shape[1])
    chip_sum, hidden_act = lax.optimization_barrier((chip_sum, hidden_act))
    hid_rows = lax.dynamic_index_in_dim(chip_sum, z, axis=0, keepdims=False)
    for s in range(1, chips):
        piece = lax.dynamic_index_in_dim(chip_sum, (z + s) % chips, axis=0, keepdims=False)
        piece = lax.ppermute(piece.astype(jnp.bfloat16), "z", shift_perm(chips, s))
        hid_rows = hid_rows + piece.astype(jnp.float32)

    gate_local = (
        hid_rows * up_float * sigmoid_gate * (1.0 + gate_float * (1.0 - sigmoid_gate))
    ).astype(jnp.bfloat16)
    up_local = (hid_rows * silu_gate).astype(jnp.bfloat16)

    acc_down = lax.dot_general(
        hidden_act, grad_full, CONTRACT_FIRST, preferred_element_type=jnp.float32
    )
    gate_delta = lax.all_gather(gate_local, ROW, axis=0, tiled=True)
    up_delta = lax.all_gather(up_local, ROW, axis=0, tiled=True)
    acc_gate = lax.dot_general(
        act_full, gate_delta, CONTRACT_FIRST, preferred_element_type=jnp.float32
    )
    input_gate = reduce_scatter_col(
        lax.dot_general(gate_delta, gate_weight, CONTRACT_LAST, preferred_element_type=jnp.float32)
    )
    acc_up = lax.dot_general(act_full, up_delta, CONTRACT_FIRST, preferred_element_type=jnp.float32)
    input_up = reduce_scatter_col(
        lax.dot_general(up_delta, up_weight, CONTRACT_LAST, preferred_element_type=jnp.float32)
    )
    input_rows = (input_gate + input_up).astype(jnp.bfloat16)
    factor = float(tokens_all) ** (-0.5)
    return (
        input_rows,
        (acc_gate * factor).astype(jnp.bfloat16),
        (acc_up * factor).astype(jnp.bfloat16),
        (acc_down * factor).astype(jnp.bfloat16),
    )


def solution(mesh):
    in_specs = (
        P("col", ROW),
        P("col", ROW),
        P(ROW, "col"),
        P(ROW, "col"),
        P(ROW, "col"),
        P(ROW, "col"),
        P("col", ROW),
    )
    out_specs = (P("col", ROW), P(ROW, "col"), P(ROW, "col"), P("col", ROW))
    devices = mesh.devices.reshape(mesh.shape["row"] // 2, 2, mesh.shape["col"])
    split_mesh = jax.sharding.Mesh(devices, ("z", "core", "col"))
    return jax.shard_map(body, mesh=split_mesh, in_specs=in_specs, out_specs=out_specs, check_vma=False)
```

```python
import jax
import jax.numpy as jnp
from jax import lax
from jax.sharding import PartitionSpec as P


CONTRACT_LAST = (((1,), (1,)), ((), ()))
CONTRACT_FIRST = (((0,), (0,)), ((), ()))
ROW = ("z", "core")


def shift_perm(n, s):
    return [(i, (i + s) % n) for i in range(n)]


def gather_col(block):
    n = lax.axis_size("col")
    c = lax.axis_index("col")
    rows = block.shape[0]
    full = jnp.zeros((n * rows,) + block.shape[1:], block.dtype)
    full = lax.dynamic_update_slice_in_dim(full, block, c * rows, axis=0)
    for s in range(1, n):
        part = lax.ppermute(block, "col", shift_perm(n, s))
        full = lax.dynamic_update_slice_in_dim(full, part, ((c - s) % n) * rows, axis=0)
    return full


def reduce_scatter_col(partial):
    n = lax.axis_size("col")
    c = lax.axis_index("col")
    blocks = partial.reshape((n, -1) + partial.shape[1:])
    total = lax.dynamic_index_in_dim(blocks, c, axis=0, keepdims=False)
    for s in range(1, n):
        piece = lax.dynamic_index_in_dim(blocks, (c + s) % n, axis=0, keepdims=False)
        total = total + lax.ppermute(piece, "col", shift_perm(n, s))
    return total


def body(activations, out_grad, gate_pre, up_proj, gate_weight, up_weight, down_weight):
    gate_float = gate_pre.astype(jnp.float32)
    up_float = up_proj.astype(jnp.float32)
    sigmoid_gate = jax.nn.sigmoid(gate_float)
    silu_gate = gate_float * sigmoid_gate
    hidden_local = (silu_gate * up_float).astype(jnp.bfloat16)
    hidden_act = lax.all_gather(hidden_local, ROW, axis=0, tiled=True)

    width = out_grad.shape[1]
    both_full = gather_col(jnp.concatenate([out_grad, activations], axis=1))
    grad_full = both_full[:, :width]
    act_full = both_full[:, width:]
    tokens_all = act_full.shape[0]

    chips = lax.axis_size("z")
    z = lax.axis_index("z")
    core = lax.axis_index("core")
    grad_blocks = grad_full.reshape(chips, 2, -1, width)
    grad_send = lax.dynamic_index_in_dim(grad_blocks, 1 - core, axis=1, keepdims=False)
    grad_keep = lax.dynamic_index_in_dim(grad_blocks, core, axis=1, keepdims=False)
    hid_send = lax.dot_general(
        grad_send.reshape(-1, width), down_weight, CONTRACT_LAST,
        preferred_element_type=jnp.float32,
    )
    hid_recv = lax.ppermute(hid_send, "core", [(0, 1), (1, 0)])
    hid_keep = lax.dot_general(
        grad_keep.reshape(-1, width), down_weight, CONTRACT_LAST,
        preferred_element_type=jnp.float32,
    )
    (hid_keep,) = lax.optimization_barrier((hid_keep,))
    chip_sum = (hid_keep + hid_recv).reshape(chips, -1, hid_keep.shape[1])
    hid_rows = lax.dynamic_index_in_dim(chip_sum, z, axis=0, keepdims=False)
    pieces = [
        lax.dynamic_index_in_dim(chip_sum, (z + s) % chips, axis=0, keepdims=False).astype(
            jnp.bfloat16
        )
        for s in range(1, chips)
    ]
    pieces, hid_rows, hidden_act = lax.optimization_barrier((pieces, hid_rows, hidden_act))
    for s, piece in enumerate(pieces, start=1):
        piece = lax.ppermute(piece, "z", shift_perm(chips, s))
        hid_rows = hid_rows + piece.astype(jnp.float32)

    gate_local = (
        hid_rows * up_float * sigmoid_gate * (1.0 + gate_float * (1.0 - sigmoid_gate))
    ).astype(jnp.bfloat16)
    up_local = (hid_rows * silu_gate).astype(jnp.bfloat16)

    acc_down = lax.dot_general(
        hidden_act, grad_full, CONTRACT_FIRST, preferred_element_type=jnp.float32
    )
    gate_delta = lax.all_gather(gate_local, ROW, axis=0, tiled=True)
    half = up_local.shape[1] // 2
    up_delta_a = lax.all_gather(up_local[:, :half], ROW, axis=0, tiled=True)
    up_delta_b = lax.all_gather(up_local[:, half:], ROW, axis=0, tiled=True)
    acc_gate = lax.dot_general(
        act_full, gate_delta, CONTRACT_FIRST, preferred_element_type=jnp.float32
    )
    input_part = lax.dot_general(
        gate_delta, gate_weight, CONTRACT_LAST, preferred_element_type=jnp.float32
    )
    input_part = input_part + lax.dot_general(
        up_delta_a, up_weight[:, :half], CONTRACT_LAST, preferred_element_type=jnp.float32
    )
    input_part = reduce_scatter_col(input_part)
    acc_up_a = lax.dot_general(
        act_full, up_delta_a, CONTRACT_FIRST, preferred_element_type=jnp.float32
    )
    acc_up_b = lax.dot_general(
        act_full, up_delta_b, CONTRACT_FIRST, preferred_element_type=jnp.float32
    )
    acc_up = jnp.concatenate([acc_up_a, acc_up_b], axis=1)
    input_rest = reduce_scatter_col(
        lax.dot_general(
            up_delta_b, up_weight[:, half:], CONTRACT_LAST, preferred_element_type=jnp.float32
        )
    )
    input_rows = (input_part + input_rest).astype(jnp.bfloat16)
    factor = float(tokens_all) ** (-0.5)
    return (
        input_rows,
        (acc_gate * factor).astype(jnp.bfloat16),
        (acc_up * factor).astype(jnp.bfloat16),
        (acc_down * factor).astype(jnp.bfloat16),
    )


def solution(mesh):
    in_specs = (
        P("col", ROW),
        P("col", ROW),
        P(ROW, "col"),
        P(ROW, "col"),
        P(ROW, "col"),
        P(ROW, "col"),
        P("col", ROW),
    )
    out_specs = (P("col", ROW), P(ROW, "col"), P(ROW, "col"), P("col", ROW))
    devices = mesh.devices.reshape(mesh.shape["row"] // 2, 2, mesh.shape["col"])
    split_mesh = jax.sharding.Mesh(devices, ("z", "core", "col"))
    return jax.shard_map(body, mesh=split_mesh, in_specs=in_specs, out_specs=out_specs, check_vma=False)
```

```python
import jax
import jax.numpy as jnp
from jax import lax
from jax.sharding import PartitionSpec as P


CONTRACT_LAST = (((1,), (1,)), ((), ()))
CONTRACT_FIRST = (((0,), (0,)), ((), ()))
ROW = ("z", "core")


def shift_perm(n, s):
    return [(i, (i + s) % n) for i in range(n)]


def gather_col(block):
    n = lax.axis_size("col")
    c = lax.axis_index("col")
    rows = block.shape[0]
    full = jnp.zeros((n * rows,) + block.shape[1:], block.dtype)
    full = lax.dynamic_update_slice_in_dim(full, block, c * rows, axis=0)
    for s in range(1, n):
        part = lax.ppermute(block, "col", shift_perm(n, s))
        full = lax.dynamic_update_slice_in_dim(full, part, ((c - s) % n) * rows, axis=0)
    return full


def gather_row(block):
    chips = lax.axis_size("z")
    z = lax.axis_index("z")
    core = lax.axis_index("core")
    rows = block.shape[0]
    mine = jnp.zeros((chips * rows,) + block.shape[1:], block.dtype)
    mine = lax.dynamic_update_slice_in_dim(mine, block, z * rows, axis=0)
    for s in range(1, chips):
        part = lax.ppermute(block, "z", shift_perm(chips, s))
        mine = lax.dynamic_update_slice_in_dim(mine, part, ((z - s) % chips) * rows, axis=0)
    other = lax.ppermute(mine, "core", [(0, 1), (1, 0)])
    pair = jnp.stack([mine, other]).reshape((2, chips, rows) + block.shape[1:])
    first = jnp.where(core == 0, pair[0], pair[1])
    second = jnp.where(core == 0, pair[1], pair[0])
    full = jnp.stack([first, second], axis=1)
    return full.reshape((2 * chips * rows,) + block.shape[1:])


def reduce_scatter_col(partial):
    n = lax.axis_size("col")
    c = lax.axis_index("col")
    blocks = partial.reshape((n, -1) + partial.shape[1:])
    total = lax.dynamic_index_in_dim(blocks, c, axis=0, keepdims=False)
    for s in range(1, n):
        piece = lax.dynamic_index_in_dim(blocks, (c + s) % n, axis=0, keepdims=False)
        total = total + lax.ppermute(piece, "col", shift_perm(n, s))
    return total


def body(activations, out_grad, gate_pre, up_proj, gate_weight, up_weight, down_weight):
    gate_float = gate_pre.astype(jnp.float32)
    up_float = up_proj.astype(jnp.float32)
    sigmoid_gate = jax.nn.sigmoid(gate_float)
    silu_gate = gate_float * sigmoid_gate
    hidden_local = (silu_gate * up_float).astype(jnp.bfloat16)
    hidden_act = lax.all_gather(hidden_local, ROW, axis=0, tiled=True)

    grad_full = gather_col(out_grad)
    activations, grad_full = lax.optimization_barrier((activations, grad_full))
    act_full = gather_col(activations)
    tokens_all = act_full.shape[0]

    chips = lax.axis_size("z")
    z = lax.axis_index("z")
    core = lax.axis_index("core")
    width = grad_full.shape[1]
    grad_blocks = grad_full.reshape(chips, 2, -1, width)
    grad_send = lax.dynamic_index_in_dim(grad_blocks, 1 - core, axis=1, keepdims=False)
    grad_keep = lax.dynamic_index_in_dim(grad_blocks, core, axis=1, keepdims=False)
    hid_send = lax.dot_general(
        grad_send.reshape(-1, width), down_weight, CONTRACT_LAST,
        preferred_element_type=jnp.float32,
    )
    hid_recv = lax.ppermute(hid_send, "core", [(0, 1), (1, 0)])
    hid_keep = lax.dot_general(
        grad_keep.reshape(-1, width), down_weight, CONTRACT_LAST,
        preferred_element_type=jnp.float32,
    )
    chip_sum = (hid_keep + hid_recv).reshape(chips, -1, hid_keep.shape[1])
    chip_sum, hidden_act, act_full = lax.optimization_barrier((chip_sum, hidden_act, act_full))
    hid_rows = lax.dynamic_index_in_dim(chip_sum, z, axis=0, keepdims=False)
    for s in range(1, chips):
        piece = lax.dynamic_index_in_dim(chip_sum, (z + s) % chips, axis=0, keepdims=False)
        piece = lax.ppermute(piece.astype(jnp.bfloat16), "z", shift_perm(chips, s))
        hid_rows = hid_rows + piece.astype(jnp.float32)

    acc_down = lax.dot_general(
        hidden_act, grad_full, CONTRACT_FIRST, preferred_element_type=jnp.float32
    )
    hid_rows, acc_down = lax.optimization_barrier((hid_rows, acc_down))
    gate_local = (
        hid_rows * up_float * sigmoid_gate * (1.0 + gate_float * (1.0 - sigmoid_gate))
    ).astype(jnp.bfloat16)
    up_local = (hid_rows * silu_gate).astype(jnp.bfloat16)

    gate_delta = lax.all_gather(gate_local, ROW, axis=0, tiled=True)
    up_delta = gather_row(up_local)
    acc_gate = lax.dot_general(
        act_full, gate_delta, CONTRACT_FIRST, preferred_element_type=jnp.float32
    )
    input_gate = reduce_scatter_col(
        lax.dot_general(gate_delta, gate_weight, CONTRACT_LAST, preferred_element_type=jnp.float32)
    )
    acc_up = lax.dot_general(act_full, up_delta, CONTRACT_FIRST, preferred_element_type=jnp.float32)
    input_up = reduce_scatter_col(
        lax.dot_general(up_delta, up_weight, CONTRACT_LAST, preferred_element_type=jnp.float32)
    )
    input_rows = (input_gate + input_up).astype(jnp.bfloat16)
    factor = float(tokens_all) ** (-0.5)
    return (
        input_rows,
        (acc_gate * factor).astype(jnp.bfloat16),
        (acc_up * factor).astype(jnp.bfloat16),
        (acc_down * factor).astype(jnp.bfloat16),
    )


def solution(mesh):
    in_specs = (
        P("col", ROW),
        P("col", ROW),
        P(ROW, "col"),
        P(ROW, "col"),
        P(ROW, "col"),
        P(ROW, "col"),
        P("col", ROW),
    )
    out_specs = (P("col", ROW), P(ROW, "col"), P(ROW, "col"), P("col", ROW))
    devices = mesh.devices.reshape(mesh.shape["row"] // 2, 2, mesh.shape["col"])
    split_mesh = jax.sharding.Mesh(devices, ("z", "core", "col"))
    return jax.shard_map(body, mesh=split_mesh, in_specs=in_specs, out_specs=out_specs, check_vma=False)
```

```python
import jax
import jax.numpy as jnp
from jax import lax
from jax.sharding import PartitionSpec as P


CONTRACT_LAST = (((1,), (1,)), ((), ()))
CONTRACT_FIRST = (((0,), (0,)), ((), ()))
ROW = ("z", "core")


def shift_perm(n, s):
    return [(i, (i + s) % n) for i in range(n)]


def gather_col(block):
    n = lax.axis_size("col")
    c = lax.axis_index("col")
    rows = block.shape[0]
    full = jnp.zeros((n * rows,) + block.shape[1:], block.dtype)
    full = lax.dynamic_update_slice_in_dim(full, block, c * rows, axis=0)
    for s in range(1, n):
        part = lax.ppermute(block, "col", shift_perm(n, s))
        full = lax.dynamic_update_slice_in_dim(full, part, ((c - s) % n) * rows, axis=0)
    return full


def reduce_scatter_col(partial):
    n = lax.axis_size("col")
    c = lax.axis_index("col")
    blocks = partial.reshape((n, -1) + partial.shape[1:])
    total = lax.dynamic_index_in_dim(blocks, c, axis=0, keepdims=False)
    for s in range(1, n):
        piece = lax.dynamic_index_in_dim(blocks, (c + s) % n, axis=0, keepdims=False)
        total = total + lax.ppermute(piece, "col", shift_perm(n, s))
    return total


def body(activations, out_grad, gate_pre, up_proj, gate_weight, up_weight, down_weight):
    gate_float = gate_pre.astype(jnp.float32)
    up_float = up_proj.astype(jnp.float32)
    sigmoid_gate = jax.nn.sigmoid(gate_float)
    silu_gate = gate_float * sigmoid_gate
    hidden_local = (silu_gate * up_float).astype(jnp.bfloat16)
    hidden_act = lax.all_gather(hidden_local, ROW, axis=0, tiled=True)

    grad_full = gather_col(out_grad)
    activations, grad_full = lax.optimization_barrier((activations, grad_full))
    act_full = gather_col(activations)
    tokens_all = act_full.shape[0]

    chips = lax.axis_size("z")
    z = lax.axis_index("z")
    core = lax.axis_index("core")
    width = grad_full.shape[1]
    grad_blocks = grad_full.reshape(chips, 2, -1, width)
    grad_send = lax.dynamic_index_in_dim(grad_blocks, 1 - core, axis=1, keepdims=False)
    grad_keep = lax.dynamic_index_in_dim(grad_blocks, core, axis=1, keepdims=False)
    hid_send = lax.dot_general(
        grad_send.reshape(-1, width), down_weight, CONTRACT_LAST,
        preferred_element_type=jnp.float32,
    )
    hid_recv = lax.ppermute(hid_send, "core", [(0, 1), (1, 0)])
    hid_keep = lax.dot_general(
        grad_keep.reshape(-1, width), down_weight, CONTRACT_LAST,
        preferred_element_type=jnp.float32,
    )
    chip_sum = (hid_keep + hid_recv).reshape(chips, -1, hid_keep.shape[1])
    hid_rows = lax.dynamic_index_in_dim(chip_sum, z, axis=0, keepdims=False)
    pieces = [
        lax.dynamic_index_in_dim(chip_sum, (z + s) % chips, axis=0, keepdims=False).astype(
            jnp.bfloat16
        )
        for s in range(1, chips)
    ]
    pieces, hid_rows, hidden_act, act_full = lax.optimization_barrier(
        (pieces, hid_rows, hidden_act, act_full)
    )
    for s, piece in enumerate(pieces, start=1):
        piece = lax.ppermute(piece, "z", shift_perm(chips, s))
        hid_rows = hid_rows + piece.astype(jnp.float32)
    acc_down = lax.dot_general(
        hidden_act, grad_full, CONTRACT_FIRST, preferred_element_type=jnp.float32
    )
    hid_rows, acc_down = lax.optimization_barrier((hid_rows, acc_down))

    gate_local = (
        hid_rows * up_float * sigmoid_gate * (1.0 + gate_float * (1.0 - sigmoid_gate))
    ).astype(jnp.bfloat16)
    up_local = (hid_rows * silu_gate).astype(jnp.bfloat16)

    gate_delta = lax.all_gather(gate_local, ROW, axis=0, tiled=True)
    up_delta = lax.all_gather(up_local, ROW, axis=0, tiled=True)
    acc_gate = lax.dot_general(
        act_full, gate_delta, CONTRACT_FIRST, preferred_element_type=jnp.float32
    )
    input_gate = reduce_scatter_col(
        lax.dot_general(gate_delta, gate_weight, CONTRACT_LAST, preferred_element_type=jnp.float32)
    )
    acc_gate, input_gate, up_delta = lax.optimization_barrier((acc_gate, input_gate, up_delta))
    acc_up = lax.dot_general(act_full, up_delta, CONTRACT_FIRST, preferred_element_type=jnp.float32)
    input_up = reduce_scatter_col(
        lax.dot_general(up_delta, up_weight, CONTRACT_LAST, preferred_element_type=jnp.float32)
    )
    input_rows = (input_gate + input_up).astype(jnp.bfloat16)
    factor = float(tokens_all) ** (-0.5)
    return (
        input_rows,
        (acc_gate * factor).astype(jnp.bfloat16),
        (acc_up * factor).astype(jnp.bfloat16),
        (acc_down * factor).astype(jnp.bfloat16),
    )


def solution(mesh):
    in_specs = (
        P("col", ROW),
        P("col", ROW),
        P(ROW, "col"),
        P(ROW, "col"),
        P(ROW, "col"),
        P(ROW, "col"),
        P("col", ROW),
    )
    out_specs = (P("col", ROW), P(ROW, "col"), P(ROW, "col"), P("col", ROW))
    devices = mesh.devices.reshape(mesh.shape["row"] // 2, 2, mesh.shape["col"])
    split_mesh = jax.sharding.Mesh(devices, ("z", "core", "col"))
    return jax.shard_map(body, mesh=split_mesh, in_specs=in_specs, out_specs=out_specs, check_vma=False)
```

```python
import jax
import jax.numpy as jnp
from jax import lax
from jax.sharding import PartitionSpec as P


CONTRACT_LAST = (((1,), (1,)), ((), ()))
CONTRACT_FIRST = (((0,), (0,)), ((), ()))
ROW = ("z", "core")


def shift_perm(n, s):
    return [(i, (i + s) % n) for i in range(n)]


def gather_col(block):
    n = lax.axis_size("col")
    c = lax.axis_index("col")
    rows = block.shape[0]
    full = jnp.zeros((n * rows,) + block.shape[1:], block.dtype)
    full = lax.dynamic_update_slice_in_dim(full, block, c * rows, axis=0)
    for s in range(1, n):
        part = lax.ppermute(block, "col", shift_perm(n, s))
        full = lax.dynamic_update_slice_in_dim(full, part, ((c - s) % n) * rows, axis=0)
    return full


def reduce_scatter_col(partial):
    n = lax.axis_size("col")
    c = lax.axis_index("col")
    blocks = partial.reshape((n, -1) + partial.shape[1:])
    total = lax.dynamic_index_in_dim(blocks, c, axis=0, keepdims=False)
    for s in range(1, n):
        piece = lax.dynamic_index_in_dim(blocks, (c + s) % n, axis=0, keepdims=False)
        total = total + lax.ppermute(piece, "col", shift_perm(n, s))
    return total


def body(activations, out_grad, gate_pre, up_proj, gate_weight, up_weight, down_weight):
    gate_float = gate_pre.astype(jnp.float32)
    up_float = up_proj.astype(jnp.float32)
    sigmoid_gate = jax.nn.sigmoid(gate_float)
    silu_gate = gate_float * sigmoid_gate
    hidden_local = (silu_gate * up_float).astype(jnp.bfloat16)
    hidden_act = lax.all_gather(hidden_local, ROW, axis=0, tiled=True)

    grad_full = gather_col(out_grad)
    activations, grad_full = lax.optimization_barrier((activations, grad_full))
    act_full = gather_col(activations)
    tokens_all = act_full.shape[0]

    chips = lax.axis_size("z")
    z = lax.axis_index("z")
    core = lax.axis_index("core")
    width = grad_full.shape[1]
    grad_blocks = grad_full.reshape(chips, 2, -1, width)
    grad_send = lax.dynamic_index_in_dim(grad_blocks, 1 - core, axis=1, keepdims=False)
    grad_keep = lax.dynamic_index_in_dim(grad_blocks, core, axis=1, keepdims=False)
    hid_send = lax.dot_general(
        grad_send.reshape(-1, width), down_weight, CONTRACT_LAST,
        preferred_element_type=jnp.float32,
    )
    hid_recv = lax.ppermute(hid_send, "core", [(0, 1), (1, 0)])
    hid_keep = lax.dot_general(
        grad_keep.reshape(-1, width), down_weight, CONTRACT_LAST,
        preferred_element_type=jnp.float32,
    )
    chip_sum = (hid_keep + hid_recv).reshape(chips, -1, hid_keep.shape[1])
    chip_sum, hidden_act, act_full = lax.optimization_barrier((chip_sum, hidden_act, act_full))
    hid_rows = lax.dynamic_index_in_dim(chip_sum, z, axis=0, keepdims=False)
    for s in range(1, chips):
        piece = lax.dynamic_index_in_dim(chip_sum, (z + s) % chips, axis=0, keepdims=False)
        piece = lax.ppermute(piece.astype(jnp.bfloat16), "z", shift_perm(chips, s))
        hid_rows = hid_rows + piece.astype(jnp.float32)
    acc_down = lax.dot_general(
        hidden_act, grad_full, CONTRACT_FIRST, preferred_element_type=jnp.float32
    )
    hid_rows, acc_down = lax.optimization_barrier((hid_rows, acc_down))

    gate_local = (
        hid_rows * up_float * sigmoid_gate * (1.0 + gate_float * (1.0 - sigmoid_gate))
    ).astype(jnp.bfloat16)
    up_local = (hid_rows * silu_gate).astype(jnp.bfloat16)

    gate_delta = lax.all_gather(gate_local, ROW, axis=0, tiled=True)
    up_delta = lax.all_gather(up_local, ROW, axis=0, tiled=True)
    acc_gate = lax.dot_general(
        act_full, gate_delta, CONTRACT_FIRST, preferred_element_type=jnp.float32
    )
    input_gate = reduce_scatter_col(
        lax.dot_general(gate_delta, gate_weight, CONTRACT_LAST, preferred_element_type=jnp.float32)
    )
    acc_gate, input_gate, up_delta = lax.optimization_barrier((acc_gate, input_gate, up_delta))
    input_up = lax.dot_general(
        up_delta, up_weight, CONTRACT_LAST, preferred_element_type=jnp.float32
    )
    up_delta, input_up = lax.optimization_barrier((up_delta, input_up))
    input_up = reduce_scatter_col(input_up)
    acc_up = lax.dot_general(act_full, up_delta, CONTRACT_FIRST, preferred_element_type=jnp.float32)
    input_rows = (input_gate + input_up).astype(jnp.bfloat16)
    factor = float(tokens_all) ** (-0.5)
    return (
        input_rows,
        (acc_gate * factor).astype(jnp.bfloat16),
        (acc_up * factor).astype(jnp.bfloat16),
        (acc_down * factor).astype(jnp.bfloat16),
    )


def solution(mesh):
    in_specs = (
        P("col", ROW),
        P("col", ROW),
        P(ROW, "col"),
        P(ROW, "col"),
        P(ROW, "col"),
        P(ROW, "col"),
        P("col", ROW),
    )
    out_specs = (P("col", ROW), P(ROW, "col"), P(ROW, "col"), P("col", ROW))
    devices = mesh.devices.reshape(mesh.shape["row"] // 2, 2, mesh.shape["col"])
    split_mesh = jax.sharding.Mesh(devices, ("z", "core", "col"))
    return jax.shard_map(body, mesh=split_mesh, in_specs=in_specs, out_specs=out_specs, check_vma=False)
```

```python
import jax
import jax.numpy as jnp
from jax import lax
from jax.sharding import PartitionSpec as P


CONTRACT_LAST = (((1,), (1,)), ((), ()))
CONTRACT_FIRST = (((0,), (0,)), ((), ()))
ROW = ("z", "core")


def shift_perm(n, s):
    return [(i, (i + s) % n) for i in range(n)]


def gather_col(block):
    n = lax.axis_size("col")
    c = lax.axis_index("col")
    rows = block.shape[0]
    full = jnp.zeros((n * rows,) + block.shape[1:], block.dtype)
    full = lax.dynamic_update_slice_in_dim(full, block, c * rows, axis=0)
    for s in range(1, n):
        part = lax.ppermute(block, "col", shift_perm(n, s))
        full = lax.dynamic_update_slice_in_dim(full, part, ((c - s) % n) * rows, axis=0)
    return full


def reduce_scatter_col(partial):
    n = lax.axis_size("col")
    c = lax.axis_index("col")
    blocks = partial.reshape((n, -1) + partial.shape[1:])
    total = lax.dynamic_index_in_dim(blocks, c, axis=0, keepdims=False)
    for s in range(1, n):
        piece = lax.dynamic_index_in_dim(blocks, (c + s) % n, axis=0, keepdims=False)
        total = total + lax.ppermute(piece, "col", shift_perm(n, s))
    return total


def body(activations, out_grad, gate_pre, up_proj, gate_weight, up_weight, down_weight):
    gate_float = gate_pre.astype(jnp.float32)
    up_float = up_proj.astype(jnp.float32)
    sigmoid_gate = jax.nn.sigmoid(gate_float)
    silu_gate = gate_float * sigmoid_gate
    hidden_local = (silu_gate * up_float).astype(jnp.bfloat16)
    hidden_act = lax.all_gather(hidden_local, ROW, axis=0, tiled=True)

    grad_full = gather_col(out_grad)
    activations, grad_full = lax.optimization_barrier((activations, grad_full))
    act_full = gather_col(activations)
    tokens_all = act_full.shape[0]

    chips = lax.axis_size("z")
    z = lax.axis_index("z")
    core = lax.axis_index("core")
    width = grad_full.shape[1]
    grad_blocks = grad_full.reshape(chips, 2, -1, width)
    grad_send = lax.dynamic_index_in_dim(grad_blocks, 1 - core, axis=1, keepdims=False)
    grad_keep = lax.dynamic_index_in_dim(grad_blocks, core, axis=1, keepdims=False)
    hid_send = lax.dot_general(
        grad_send.reshape(-1, width), down_weight, CONTRACT_LAST,
        preferred_element_type=jnp.float32,
    )
    hid_recv = lax.ppermute(hid_send, "core", [(0, 1), (1, 0)])
    hid_keep = lax.dot_general(
        grad_keep.reshape(-1, width), down_weight, CONTRACT_LAST,
        preferred_element_type=jnp.float32,
    )
    chip_sum = (hid_keep + hid_recv).reshape(chips, -1, hid_keep.shape[1])
    chip_sum, hidden_act, act_full = lax.optimization_barrier((chip_sum, hidden_act, act_full))
    hid_rows = lax.dynamic_index_in_dim(chip_sum, z, axis=0, keepdims=False)
    for s in range(1, chips):
        piece = lax.dynamic_index_in_dim(chip_sum, (z + s) % chips, axis=0, keepdims=False)
        piece = lax.ppermute(piece.astype(jnp.bfloat16), "z", shift_perm(chips, s))
        hid_rows = hid_rows + piece.astype(jnp.float32)

    gate_local = (
        hid_rows * up_float * sigmoid_gate * (1.0 + gate_float * (1.0 - sigmoid_gate))
    ).astype(jnp.bfloat16)
    up_local = (hid_rows * silu_gate).astype(jnp.bfloat16)

    acc_down = lax.dot_general(
        hidden_act, grad_full, CONTRACT_FIRST, preferred_element_type=jnp.float32
    )
    gate_delta = lax.all_gather(gate_local, ROW, axis=0, tiled=True)
    up_delta = lax.all_gather(up_local, ROW, axis=0, tiled=True)
    acc_gate = lax.dot_general(
        act_full, gate_delta, CONTRACT_FIRST, preferred_element_type=jnp.float32
    )
    input_gate = reduce_scatter_col(
        lax.dot_general(gate_delta, gate_weight, CONTRACT_LAST, preferred_element_type=jnp.float32)
    )
    acc_gate, input_gate, up_delta = lax.optimization_barrier((acc_gate, input_gate, up_delta))
    input_up = lax.dot_general(
        up_delta, up_weight, CONTRACT_LAST, preferred_element_type=jnp.float32
    )
    up_delta, input_up = lax.optimization_barrier((up_delta, input_up))
    input_up = reduce_scatter_col(input_up)
    acc_up = lax.dot_general(act_full, up_delta, CONTRACT_FIRST, preferred_element_type=jnp.float32)
    input_rows = (input_gate + input_up).astype(jnp.bfloat16)
    factor = float(tokens_all) ** (-0.5)
    return (
        input_rows,
        (acc_gate * factor).astype(jnp.bfloat16),
        (acc_up * factor).astype(jnp.bfloat16),
        (acc_down * factor).astype(jnp.bfloat16),
    )


def solution(mesh):
    in_specs = (
        P("col", ROW),
        P("col", ROW),
        P(ROW, "col"),
        P(ROW, "col"),
        P(ROW, "col"),
        P(ROW, "col"),
        P("col", ROW),
    )
    out_specs = (P("col", ROW), P(ROW, "col"), P(ROW, "col"), P("col", ROW))
    devices = mesh.devices.reshape(mesh.shape["row"] // 2, 2, mesh.shape["col"])
    split_mesh = jax.sharding.Mesh(devices, ("z", "core", "col"))
    return jax.shard_map(body, mesh=split_mesh, in_specs=in_specs, out_specs=out_specs, check_vma=False)
```

```python
import jax
import jax.numpy as jnp
from jax import lax
from jax.sharding import PartitionSpec as P


CONTRACT_LAST = (((1,), (1,)), ((), ()))
CONTRACT_FIRST = (((0,), (0,)), ((), ()))
ROW = ("z", "core")


def shift_perm(n, s):
    return [(i, (i + s) % n) for i in range(n)]


def gather_col(block):
    n = lax.axis_size("col")
    c = lax.axis_index("col")
    rows = block.shape[0]
    full = jnp.zeros((n * rows,) + block.shape[1:], block.dtype)
    full = lax.dynamic_update_slice_in_dim(full, block, c * rows, axis=0)
    for s in range(1, n):
        part = lax.ppermute(block, "col", shift_perm(n, s))
        full = lax.dynamic_update_slice_in_dim(full, part, ((c - s) % n) * rows, axis=0)
    return full


def reduce_scatter_col(partial, send_dtype=jnp.float32):
    n = lax.axis_size("col")
    c = lax.axis_index("col")
    blocks = partial.reshape((n, -1) + partial.shape[1:])
    total = lax.dynamic_index_in_dim(blocks, c, axis=0, keepdims=False)
    for s in range(1, n):
        piece = lax.dynamic_index_in_dim(blocks, (c + s) % n, axis=0, keepdims=False)
        piece = lax.ppermute(piece.astype(send_dtype), "col", shift_perm(n, s))
        total = total + piece.astype(jnp.float32)
    return total


def body(activations, out_grad, gate_pre, up_proj, gate_weight, up_weight, down_weight):
    gate_float = gate_pre.astype(jnp.float32)
    up_float = up_proj.astype(jnp.float32)
    sigmoid_gate = jax.nn.sigmoid(gate_float)
    silu_gate = gate_float * sigmoid_gate
    hidden_local = (silu_gate * up_float).astype(jnp.bfloat16)
    hidden_act = lax.all_gather(hidden_local, ROW, axis=0, tiled=True)

    grad_full = gather_col(out_grad)
    activations, grad_full = lax.optimization_barrier((activations, grad_full))
    act_full = gather_col(activations)
    tokens_all = act_full.shape[0]

    chips = lax.axis_size("z")
    z = lax.axis_index("z")
    core = lax.axis_index("core")
    width = grad_full.shape[1]
    grad_blocks = grad_full.reshape(chips, 2, -1, width)
    grad_send = lax.dynamic_index_in_dim(grad_blocks, 1 - core, axis=1, keepdims=False)
    grad_keep = lax.dynamic_index_in_dim(grad_blocks, core, axis=1, keepdims=False)
    hid_send = lax.dot_general(
        grad_send.reshape(-1, width), down_weight, CONTRACT_LAST,
        preferred_element_type=jnp.float32,
    )
    hid_recv = lax.ppermute(hid_send, "core", [(0, 1), (1, 0)])
    hid_keep = lax.dot_general(
        grad_keep.reshape(-1, width), down_weight, CONTRACT_LAST,
        preferred_element_type=jnp.float32,
    )
    chip_sum = (hid_keep + hid_recv).reshape(chips, -1, hid_keep.shape[1])
    chip_sum, hidden_act, act_full = lax.optimization_barrier((chip_sum, hidden_act, act_full))
    hid_rows = lax.dynamic_index_in_dim(chip_sum, z, axis=0, keepdims=False)
    for s in range(1, chips):
        piece = lax.dynamic_index_in_dim(chip_sum, (z + s) % chips, axis=0, keepdims=False)
        piece = lax.ppermute(piece.astype(jnp.bfloat16), "z", shift_perm(chips, s))
        hid_rows = hid_rows + piece.astype(jnp.float32)

    gate_local = (
        hid_rows * up_float * sigmoid_gate * (1.0 + gate_float * (1.0 - sigmoid_gate))
    ).astype(jnp.bfloat16)
    up_local = (hid_rows * silu_gate).astype(jnp.bfloat16)

    acc_down = lax.dot_general(
        hidden_act, grad_full, CONTRACT_FIRST, preferred_element_type=jnp.float32
    )
    gate_delta = lax.all_gather(gate_local, ROW, axis=0, tiled=True)
    up_delta = lax.all_gather(up_local, ROW, axis=0, tiled=True)
    acc_gate = lax.dot_general(
        act_full, gate_delta, CONTRACT_FIRST, preferred_element_type=jnp.float32
    )
    input_gate = reduce_scatter_col(
        lax.dot_general(gate_delta, gate_weight, CONTRACT_LAST, preferred_element_type=jnp.float32)
    )
    acc_gate, input_gate, up_delta = lax.optimization_barrier((acc_gate, input_gate, up_delta))
    input_up = lax.dot_general(
        up_delta, up_weight, CONTRACT_LAST, preferred_element_type=jnp.float32
    )
    up_delta, input_up = lax.optimization_barrier((up_delta, input_up))
    input_up = reduce_scatter_col(input_up, jnp.bfloat16)
    acc_up = lax.dot_general(act_full, up_delta, CONTRACT_FIRST, preferred_element_type=jnp.float32)
    input_rows = (input_gate + input_up).astype(jnp.bfloat16)
    factor = float(tokens_all) ** (-0.5)
    return (
        input_rows,
        (acc_gate * factor).astype(jnp.bfloat16),
        (acc_up * factor).astype(jnp.bfloat16),
        (acc_down * factor).astype(jnp.bfloat16),
    )


def solution(mesh):
    in_specs = (
        P("col", ROW),
        P("col", ROW),
        P(ROW, "col"),
        P(ROW, "col"),
        P(ROW, "col"),
        P(ROW, "col"),
        P("col", ROW),
    )
    out_specs = (P("col", ROW), P(ROW, "col"), P(ROW, "col"), P("col", ROW))
    devices = mesh.devices.reshape(mesh.shape["row"] // 2, 2, mesh.shape["col"])
    split_mesh = jax.sharding.Mesh(devices, ("z", "core", "col"))
    return jax.shard_map(body, mesh=split_mesh, in_specs=in_specs, out_specs=out_specs, check_vma=False)
```

```python
import jax
import jax.numpy as jnp
from jax import lax
from jax.sharding import PartitionSpec as P


CONTRACT_LAST = (((1,), (1,)), ((), ()))
CONTRACT_FIRST = (((0,), (0,)), ((), ()))
ROW = ("z", "core")


def shift_perm(n, s):
    return [(i, (i + s) % n) for i in range(n)]


def gather_col(block):
    n = lax.axis_size("col")
    c = lax.axis_index("col")
    rows = block.shape[0]
    full = jnp.zeros((n * rows,) + block.shape[1:], block.dtype)
    full = lax.dynamic_update_slice_in_dim(full, block, c * rows, axis=0)
    for s in range(1, n):
        part = lax.ppermute(block, "col", shift_perm(n, s))
        full = lax.dynamic_update_slice_in_dim(full, part, ((c - s) % n) * rows, axis=0)
    return full


def reduce_scatter_col(partial, send_dtype=jnp.float32):
    n = lax.axis_size("col")
    c = lax.axis_index("col")
    blocks = partial.reshape((n, -1) + partial.shape[1:])
    total = lax.dynamic_index_in_dim(blocks, c, axis=0, keepdims=False)
    for s in range(1, n):
        piece = lax.dynamic_index_in_dim(blocks, (c + s) % n, axis=0, keepdims=False)
        piece = lax.ppermute(piece.astype(send_dtype), "col", shift_perm(n, s))
        total = total + piece.astype(jnp.float32)
    return total


def body(activations, out_grad, gate_pre, up_proj, gate_weight, up_weight, down_weight):
    gate_float = gate_pre.astype(jnp.float32)
    up_float = up_proj.astype(jnp.float32)
    sigmoid_gate = jax.nn.sigmoid(gate_float)
    silu_gate = gate_float * sigmoid_gate
    hidden_local = (silu_gate * up_float).astype(jnp.bfloat16)
    hidden_act = lax.all_gather(hidden_local, ROW, axis=0, tiled=True)

    grad_full = gather_col(out_grad)
    activations, grad_full = lax.optimization_barrier((activations, grad_full))
    act_full = gather_col(activations)
    tokens_all = act_full.shape[0]

    chips = lax.axis_size("z")
    z = lax.axis_index("z")
    core = lax.axis_index("core")
    width = grad_full.shape[1]
    grad_blocks = grad_full.reshape(chips, 2, -1, width)
    grad_send = lax.dynamic_index_in_dim(grad_blocks, 1 - core, axis=1, keepdims=False)
    grad_keep = lax.dynamic_index_in_dim(grad_blocks, core, axis=1, keepdims=False)
    hid_send = lax.dot_general(
        grad_send.reshape(-1, width), down_weight, CONTRACT_LAST,
        preferred_element_type=jnp.float32,
    )
    hid_recv = lax.ppermute(hid_send, "core", [(0, 1), (1, 0)])
    hid_keep = lax.dot_general(
        grad_keep.reshape(-1, width), down_weight, CONTRACT_LAST,
        preferred_element_type=jnp.float32,
    )
    chip_sum = (hid_keep + hid_recv).reshape(chips, -1, hid_keep.shape[1])
    chip_sum, hidden_act, act_full = lax.optimization_barrier((chip_sum, hidden_act, act_full))
    hid_rows = lax.dynamic_index_in_dim(chip_sum, z, axis=0, keepdims=False)
    for s in [1] + list(range(chips - 1, 1, -1)):
        piece = lax.dynamic_index_in_dim(chip_sum, (z + s) % chips, axis=0, keepdims=False)
        piece = lax.ppermute(piece.astype(jnp.bfloat16), "z", shift_perm(chips, s))
        hid_rows = hid_rows + piece.astype(jnp.float32)

    gate_local = (
        hid_rows * up_float * sigmoid_gate * (1.0 + gate_float * (1.0 - sigmoid_gate))
    ).astype(jnp.bfloat16)
    up_local = (hid_rows * silu_gate).astype(jnp.bfloat16)

    acc_down = lax.dot_general(
        hidden_act, grad_full, CONTRACT_FIRST, preferred_element_type=jnp.float32
    )
    gate_delta = lax.all_gather(gate_local, ROW, axis=0, tiled=True)
    up_delta = lax.all_gather(up_local, ROW, axis=0, tiled=True)
    acc_gate = lax.dot_general(
        act_full, gate_delta, CONTRACT_FIRST, preferred_element_type=jnp.float32
    )
    input_gate = reduce_scatter_col(
        lax.dot_general(gate_delta, gate_weight, CONTRACT_LAST, preferred_element_type=jnp.float32)
    )
    acc_gate, input_gate, up_delta = lax.optimization_barrier((acc_gate, input_gate, up_delta))
    input_up = lax.dot_general(
        up_delta, up_weight, CONTRACT_LAST, preferred_element_type=jnp.float32
    )
    up_delta, input_up = lax.optimization_barrier((up_delta, input_up))
    input_up = reduce_scatter_col(input_up, jnp.bfloat16)
    acc_up = lax.dot_general(act_full, up_delta, CONTRACT_FIRST, preferred_element_type=jnp.float32)
    input_rows = (input_gate + input_up).astype(jnp.bfloat16)
    factor = float(tokens_all) ** (-0.5)
    return (
        input_rows,
        (acc_gate * factor).astype(jnp.bfloat16),
        (acc_up * factor).astype(jnp.bfloat16),
        (acc_down * factor).astype(jnp.bfloat16),
    )


def solution(mesh):
    in_specs = (
        P("col", ROW),
        P("col", ROW),
        P(ROW, "col"),
        P(ROW, "col"),
        P(ROW, "col"),
        P(ROW, "col"),
        P("col", ROW),
    )
    out_specs = (P("col", ROW), P(ROW, "col"), P(ROW, "col"), P("col", ROW))
    devices = mesh.devices.reshape(mesh.shape["row"] // 2, 2, mesh.shape["col"])
    split_mesh = jax.sharding.Mesh(devices, ("z", "core", "col"))
    return jax.shard_map(body, mesh=split_mesh, in_specs=in_specs, out_specs=out_specs, check_vma=False)
```

```python
import jax
import jax.numpy as jnp
from jax import lax
from jax.sharding import PartitionSpec as P


CONTRACT_LAST = (((1,), (1,)), ((), ()))
CONTRACT_FIRST = (((0,), (0,)), ((), ()))
ROW = ("z", "core")


def shift_perm(n, s):
    return [(i, (i + s) % n) for i in range(n)]


def gather_col(block):
    n = lax.axis_size("col")
    c = lax.axis_index("col")
    rows = block.shape[0]
    full = jnp.zeros((n * rows,) + block.shape[1:], block.dtype)
    full = lax.dynamic_update_slice_in_dim(full, block, c * rows, axis=0)
    for s in range(1, n):
        part = lax.ppermute(block, "col", shift_perm(n, s))
        full = lax.dynamic_update_slice_in_dim(full, part, ((c - s) % n) * rows, axis=0)
    return full


def reduce_scatter_col(partial, send_dtype=jnp.float32):
    n = lax.axis_size("col")
    c = lax.axis_index("col")
    blocks = partial.reshape((n, -1) + partial.shape[1:])
    total = lax.dynamic_index_in_dim(blocks, c, axis=0, keepdims=False)
    for s in range(1, n):
        piece = lax.dynamic_index_in_dim(blocks, (c + s) % n, axis=0, keepdims=False)
        piece = lax.ppermute(piece.astype(send_dtype), "col", shift_perm(n, s))
        total = total + piece.astype(jnp.float32)
    return total


def body(activations, out_grad, gate_pre, up_proj, gate_weight, up_weight, down_weight):
    gate_float = gate_pre.astype(jnp.float32)
    up_float = up_proj.astype(jnp.float32)
    sigmoid_gate = jax.nn.sigmoid(gate_float)
    silu_gate = gate_float * sigmoid_gate
    hidden_local = (silu_gate * up_float).astype(jnp.bfloat16)
    hidden_act = lax.all_gather(hidden_local, ROW, axis=0, tiled=True)

    grad_full = gather_col(out_grad)
    activations, grad_full = lax.optimization_barrier((activations, grad_full))
    act_full = gather_col(activations)
    tokens_all = act_full.shape[0]

    chips = lax.axis_size("z")
    z = lax.axis_index("z")
    core = lax.axis_index("core")
    width = grad_full.shape[1]
    grad_blocks = grad_full.reshape(chips, 2, -1, width)
    grad_send = lax.dynamic_index_in_dim(grad_blocks, 1 - core, axis=1, keepdims=False)
    grad_keep = lax.dynamic_index_in_dim(grad_blocks, core, axis=1, keepdims=False)
    hid_send = lax.dot_general(
        grad_send.reshape(-1, width), down_weight, CONTRACT_LAST,
        preferred_element_type=jnp.float32,
    )
    hid_recv = lax.ppermute(hid_send, "core", [(0, 1), (1, 0)])
    hid_keep = lax.dot_general(
        grad_keep.reshape(-1, width), down_weight, CONTRACT_LAST,
        preferred_element_type=jnp.float32,
    )
    chip_sum = (hid_keep + hid_recv).reshape(chips, -1, hid_keep.shape[1])
    chip_sum, hidden_act, act_full = lax.optimization_barrier((chip_sum, hidden_act, act_full))
    hid_rows = lax.dynamic_index_in_dim(chip_sum, z, axis=0, keepdims=False)
    for s in [1] + list(range(chips - 1, 1, -1)):
        piece = lax.dynamic_index_in_dim(chip_sum, (z + s) % chips, axis=0, keepdims=False)
        piece = lax.ppermute(piece.astype(jnp.bfloat16), "z", shift_perm(chips, s))
        hid_rows = hid_rows + piece.astype(jnp.float32)

    gate_local = (
        hid_rows * up_float * sigmoid_gate * (1.0 + gate_float * (1.0 - sigmoid_gate))
    ).astype(jnp.bfloat16)
    up_local = (hid_rows * silu_gate).astype(jnp.bfloat16)

    acc_down = lax.dot_general(
        hidden_act, grad_full, CONTRACT_FIRST, preferred_element_type=jnp.float32
    )
    gate_delta = lax.all_gather(gate_local, ROW, axis=0, tiled=True)
    up_delta = lax.all_gather(up_local, ROW, axis=0, tiled=True)
    acc_gate = lax.dot_general(
        act_full, gate_delta, CONTRACT_FIRST, preferred_element_type=jnp.float32
    )
    input_gate = reduce_scatter_col(
        lax.dot_general(gate_delta, gate_weight, CONTRACT_LAST, preferred_element_type=jnp.float32)
    )
    factor = float(tokens_all) ** (-0.5)
    gate_grad = (acc_gate * factor).astype(jnp.bfloat16)
    gate_grad, input_gate, up_delta = lax.optimization_barrier((gate_grad, input_gate, up_delta))
    input_up = lax.dot_general(
        up_delta, up_weight, CONTRACT_LAST, preferred_element_type=jnp.float32
    )
    up_delta, input_up = lax.optimization_barrier((up_delta, input_up))
    input_up = reduce_scatter_col(input_up, jnp.bfloat16)
    acc_up = lax.dot_general(act_full, up_delta, CONTRACT_FIRST, preferred_element_type=jnp.float32)
    input_rows = (input_gate + input_up).astype(jnp.bfloat16)
    return (
        input_rows,
        gate_grad,
        (acc_up * factor).astype(jnp.bfloat16),
        (acc_down * factor).astype(jnp.bfloat16),
    )


def solution(mesh):
    in_specs = (
        P("col", ROW),
        P("col", ROW),
        P(ROW, "col"),
        P(ROW, "col"),
        P(ROW, "col"),
        P(ROW, "col"),
        P("col", ROW),
    )
    out_specs = (P("col", ROW), P(ROW, "col"), P(ROW, "col"), P("col", ROW))
    devices = mesh.devices.reshape(mesh.shape["row"] // 2, 2, mesh.shape["col"])
    split_mesh = jax.sharding.Mesh(devices, ("z", "core", "col"))
    return jax.shard_map(body, mesh=split_mesh, in_specs=in_specs, out_specs=out_specs, check_vma=False)
```

```python
import jax
import jax.numpy as jnp
from jax import lax
from jax.sharding import PartitionSpec as P


CONTRACT_LAST = (((1,), (1,)), ((), ()))
CONTRACT_FIRST = (((0,), (0,)), ((), ()))
ROW = ("z", "core")


def shift_perm(n, s):
    return [(i, (i + s) % n) for i in range(n)]


def gather_col(block):
    n = lax.axis_size("col")
    c = lax.axis_index("col")
    rows = block.shape[0]
    full = jnp.zeros((n * rows,) + block.shape[1:], block.dtype)
    full = lax.dynamic_update_slice_in_dim(full, block, c * rows, axis=0)
    for s in range(1, n):
        part = lax.ppermute(block, "col", shift_perm(n, s))
        full = lax.dynamic_update_slice_in_dim(full, part, ((c - s) % n) * rows, axis=0)
    return full


def reduce_scatter_col(partial, send_dtype=jnp.float32):
    n = lax.axis_size("col")
    c = lax.axis_index("col")
    blocks = partial.reshape((n, -1) + partial.shape[1:])
    total = lax.dynamic_index_in_dim(blocks, c, axis=0, keepdims=False)
    for s in range(1, n):
        piece = lax.dynamic_index_in_dim(blocks, (c + s) % n, axis=0, keepdims=False)
        piece = lax.ppermute(piece.astype(send_dtype), "col", shift_perm(n, s))
        total = total + piece.astype(jnp.float32)
    return total


def body(activations, out_grad, gate_pre, up_proj, gate_weight, up_weight, down_weight):
    gate_float = gate_pre.astype(jnp.float32)
    up_float = up_proj.astype(jnp.float32)
    sigmoid_gate = jax.nn.sigmoid(gate_float)
    silu_gate = gate_float * sigmoid_gate
    hidden_local = (silu_gate * up_float).astype(jnp.bfloat16)
    hidden_act = lax.all_gather(hidden_local, ROW, axis=0, tiled=True)

    grad_full = gather_col(out_grad)
    activations, grad_full = lax.optimization_barrier((activations, grad_full))
    act_full = gather_col(activations)
    tokens_all = act_full.shape[0]

    chips = lax.axis_size("z")
    z = lax.axis_index("z")
    core = lax.axis_index("core")
    width = grad_full.shape[1]
    grad_blocks = grad_full.reshape(chips, 2, -1, width)
    grad_send = lax.dynamic_index_in_dim(grad_blocks, 1 - core, axis=1, keepdims=False)
    grad_keep = lax.dynamic_index_in_dim(grad_blocks, core, axis=1, keepdims=False)
    hid_send = lax.dot_general(
        grad_send.reshape(-1, width), down_weight, CONTRACT_LAST,
        preferred_element_type=jnp.float32,
    )
    hid_recv = lax.ppermute(hid_send, "core", [(0, 1), (1, 0)])
    hid_keep = lax.dot_general(
        grad_keep.reshape(-1, width), down_weight, CONTRACT_LAST,
        preferred_element_type=jnp.float32,
    )
    chip_sum = (hid_keep + hid_recv).reshape(chips, -1, hid_keep.shape[1])
    chip_sum, hidden_act, act_full = lax.optimization_barrier((chip_sum, hidden_act, act_full))
    hid_rows = lax.dynamic_index_in_dim(chip_sum, z, axis=0, keepdims=False)
    for s in [1] + list(range(chips - 1, 1, -1)):
        piece = lax.dynamic_index_in_dim(chip_sum, (z + s) % chips, axis=0, keepdims=False)
        piece = lax.ppermute(piece.astype(jnp.bfloat16), "z", shift_perm(chips, s))
        hid_rows = hid_rows + piece.astype(jnp.float32)

    gate_local = (
        hid_rows * up_float * sigmoid_gate * (1.0 + gate_float * (1.0 - sigmoid_gate))
    ).astype(jnp.bfloat16)
    gate_local, hid_rows = lax.optimization_barrier((gate_local, hid_rows))
    up_local = (hid_rows * silu_gate).astype(jnp.bfloat16)

    acc_down = lax.dot_general(
        hidden_act, grad_full, CONTRACT_FIRST, preferred_element_type=jnp.float32
    )
    gate_delta = lax.all_gather(gate_local, ROW, axis=0, tiled=True)
    up_delta = lax.all_gather(up_local, ROW, axis=0, tiled=True)
    acc_gate = lax.dot_general(
        act_full, gate_delta, CONTRACT_FIRST, preferred_element_type=jnp.float32
    )
    input_gate = reduce_scatter_col(
        lax.dot_general(gate_delta, gate_weight, CONTRACT_LAST, preferred_element_type=jnp.float32)
    )
    acc_gate, input_gate, up_delta = lax.optimization_barrier((acc_gate, input_gate, up_delta))
    input_up = lax.dot_general(
        up_delta, up_weight, CONTRACT_LAST, preferred_element_type=jnp.float32
    )
    up_delta, input_up = lax.optimization_barrier((up_delta, input_up))
    input_up = reduce_scatter_col(input_up, jnp.bfloat16)
    acc_up = lax.dot_general(act_full, up_delta, CONTRACT_FIRST, preferred_element_type=jnp.float32)
    input_rows = (input_gate + input_up).astype(jnp.bfloat16)
    factor = float(tokens_all) ** (-0.5)
    return (
        input_rows,
        (acc_gate * factor).astype(jnp.bfloat16),
        (acc_up * factor).astype(jnp.bfloat16),
        (acc_down * factor).astype(jnp.bfloat16),
    )


def solution(mesh):
    in_specs = (
        P("col", ROW),
        P("col", ROW),
        P(ROW, "col"),
        P(ROW, "col"),
        P(ROW, "col"),
        P(ROW, "col"),
        P("col", ROW),
    )
    out_specs = (P("col", ROW), P(ROW, "col"), P(ROW, "col"), P("col", ROW))
    devices = mesh.devices.reshape(mesh.shape["row"] // 2, 2, mesh.shape["col"])
    split_mesh = jax.sharding.Mesh(devices, ("z", "core", "col"))
    return jax.shard_map(body, mesh=split_mesh, in_specs=in_specs, out_specs=out_specs, check_vma=False)
```
